256 devices in a mesh: pts: 128 (over x, y, z), rank: 2 (over core).
Axes of the slice: x: 4, y: 4, z: 8, core: 2. Of those that a mesh axis runs over, the one named last changes fastest.
Arguments:
- points: bfloat16 [131072, 256], P('pts', 'rank'), may hold values from -6 to 6
- prior: float32 [131072, 1024], P('pts', 'rank'), may hold values from -0.125 to 0.125
- first_pivots: int32 [256], replicated, may hold values from 0 to 131071, as said below
- second_pivots: int32 [256], replicated, may hold values from 0 to 131071, as said below
Outputs:
- first_columns: float32 [131072, 256], P('pts', 'rank')
- second_columns: float32 [131072, 256], P('pts', 'rank')
The draws below stay inside these ranges and needn't reach their ends.
Inputs may be any that keep to these rules, and one draw needn't show every extreme that they name: `first_pivots`: the 256 entries are distinct, and none of them is in second_pivots. `second_pivots`: the 256 entries are distinct, and none of them is in first_pivots.
All inputs are finite; a program needn't handle non-finite values.
Results may differ from the reference program's by a relative error of at most 0.0003.
Values sent between devices are 32-bit elements; how exact they have to be, the bound alone decides.
No kernel may reach another device: no remote copies, remote signals or barrier semaphores. Data moves between devices by JAX's collectives and lax.ppermute only.
A program may use at most 64 MiB of HBM per device.

```python
import jax
import jax.numpy as jnp
from jax import lax

DF = 256
R0 = 1024
B = 256
NPTS = 131072


def pivot_pair(key):
    folded = jax.random.fold_in(key, 11)
    subkeys = jax.random.split(folded, 3)
    middle = 1 + jax.random.permutation(subkeys[0], NPTS - 2)[:2 * B - 2].astype(jnp.int32)
    leading = jnp.concatenate([jnp.array([NPTS - 1], dtype=jnp.int32), middle[:B - 1]])
    trailing = jnp.concatenate([jnp.array([0], dtype=jnp.int32), middle[B - 1:]])
    leading = jnp.roll(leading, jax.random.randint(subkeys[1], (), 0, B))
    trailing = jnp.roll(trailing, jax.random.randint(subkeys[2], (), 0, B))
    return (leading, trailing)


def draw_first_pivots(key, part):
    return pivot_pair(key)[0]


def draw_second_pivots(key, part):
    return pivot_pair(key)[1]


def block_scale(stream_key, shape, cuts, low, top_value):
    level, own = 1.0, jax.random.fold_in(stream_key, 6)
    for dim, shards_of in cuts:
        draws = jnp.exp(jax.random.uniform(jax.random.fold_in(own, dim), (shards_of,), jnp.float32, low / len(cuts), top_value / len(cuts)))
        level = level * jnp.repeat(draws, shape[dim] // shards_of).reshape([-1 if axis == dim else 1 for axis in range(len(shape))])
    return level


def scatter_about(own_key, shape, spread, most, cuts=(), held_as=jnp.bfloat16):
    factor_of = block_scale(own_key, shape, cuts, -0.22, 0.18) if cuts else 1.0
    result = jax.random.normal(own_key, shape, jnp.float32) * spread * factor_of
    return jnp.minimum(jnp.maximum(result, -most), most).astype(held_as)


def setup_inputs(seed: int = 0) -> dict:
    keys = jax.random.split(jax.random.key(seed), 5)
    return {
        "points": scatter_about(keys[0], (NPTS, DF), 1.0, 6.0, ((0, 128), (1, 2))),
        "prior": scatter_about(keys[1], (NPTS, R0), (2 * R0) ** -0.5, 0.125, ((0, 128), (1, 2)), jnp.float32),
        "first_pivots": draw_first_pivots(jax.random.fold_in(keys[4], 71), 0),
        "second_pivots": draw_second_pivots(jax.random.fold_in(keys[4], 71), 0),
    }


NUGGET = 2.0

def contract(left_rows, right_rows):
    return lax.dot_general(left_rows.astype(jnp.float32), right_rows.astype(jnp.float32), (((1,), (1,)), ((), ())), precision=lax.Precision.HIGHEST, preferred_element_type=jnp.float32)

def kernel_panel(points, row_norms, prior, pivots):
    piv_x = jnp.take(points, pivots, axis=0)
    cross = lax.dot_general(points.astype(jnp.float32), piv_x.astype(jnp.float32), (((1,), (1,)), ((), ())), preferred_element_type=jnp.float32)
    distance = row_norms[:, None] + jnp.take(row_norms, pivots)[None, :] - 2.0 * cross
    global_ids = jnp.arange(points.shape[0], dtype=jnp.int32)
    matches = (global_ids[:, None] == pivots[None, :]).astype(jnp.float32)
    return jnp.exp(-distance / DF) + NUGGET * matches - contract(prior, jnp.take(prior, pivots, axis=0))

def inverse_factor(kernel_block):
    lower_factor = jnp.linalg.cholesky(kernel_block)
    identity = jnp.eye(kernel_block.shape[0], dtype=jnp.float32)
    return jax.scipy.linalg.solve_triangular(lower_factor, identity, lower=True)

def reference(points, prior, first_pivots, second_pivots):
    wide = points.astype(jnp.float32)
    row_norms = jnp.sum(wide * wide, axis=1)
    first_panel = kernel_panel(points, row_norms, prior, first_pivots)
    first_inverse = inverse_factor(jnp.take(first_panel, first_pivots, axis=0))
    first_columns = contract(first_panel, first_inverse)
    second_panel = kernel_panel(points, row_norms, prior, second_pivots) - contract(first_columns, jnp.take(first_columns, second_pivots, axis=0))
    second_inverse = inverse_factor(jnp.take(second_panel, second_pivots, axis=0))
    second_columns = contract(second_panel, second_inverse)
    return (first_columns, second_columns)
```

```python
import jax
import jax.numpy as jnp
from jax import lax
from jax.sharding import PartitionSpec as P

NUGGET = 2.0


def contract(left_rows, right_rows, precise):
    dims = (((1,), (1,)), ((), ()))
    if precise:
        return lax.dot_general(
            left_rows,
            right_rows,
            dims,
            precision=lax.Precision.HIGHEST,
            preferred_element_type=jnp.float32,
        )
    return lax.dot_general(left_rows, right_rows, dims, preferred_element_type=jnp.float32)


def owned_rows(source, pivots, first_id):
    row_count = source.shape[0]
    local_index = pivots - first_id
    inside = (local_index >= 0) & (local_index < row_count)
    picked = jnp.take(source, jnp.clip(local_index, 0, row_count - 1), axis=0)
    return jnp.where(inside[:, None], picked.astype(jnp.float32), 0.0)


def square_norms(values):
    wide = values.astype(jnp.float32)
    return jnp.sum(wide * wide, axis=1)


def distance_part(left_rows, left_norms, right_rows, right_norms):
    return left_norms[:, None] + right_norms[None, :] - 2.0 * contract(left_rows, right_rows, False)


def inverse_factor(kernel_block):
    lower_factor = jnp.linalg.cholesky(kernel_block)
    identity = jnp.eye(kernel_block.shape[0], dtype=jnp.float32)
    return jax.scipy.linalg.solve_triangular(lower_factor, identity, lower=True)


def per_device(points, prior, first_pivots, second_pivots):
    row_count, x_half = points.shape
    f_half = prior.shape[1]
    first_id = lax.axis_index("pts") * row_count
    global_ids = first_id + lax.iota(jnp.int32, row_count)
    rank = lax.axis_index("rank")
    rank_count = lax.axis_size("rank")
    block = first_pivots.shape[0]
    col_count = block // rank_count
    col_start = rank * col_count
    feature_count = x_half * rank_count
    pivots = jnp.concatenate([first_pivots, second_pivots])
    row_norms = square_norms(points)
    x_slot = jnp.zeros((2 * block, feature_count), jnp.float32)
    f_slot = jnp.zeros((2 * block, f_half * rank_count), jnp.float32)
    x_slot = lax.dynamic_update_slice_in_dim(x_slot, owned_rows(points, pivots, first_id), rank * x_half, 1)
    f_slot = lax.dynamic_update_slice_in_dim(f_slot, owned_rows(prior, pivots, first_id), rank * f_half, 1)
    x_full, f_full = lax.psum((x_slot, f_slot), ("pts", "rank"))
    x_wide = x_full.astype(jnp.bfloat16)
    full_norms = square_norms(x_full)
    piv_distance = distance_part(x_wide, full_norms, x_wide, full_norms)
    identity = jnp.eye(2 * block, dtype=jnp.float32)
    piv_kernel = jnp.exp(-piv_distance / feature_count) + NUGGET * identity - contract(f_full, f_full, True)
    first_inverse = inverse_factor(piv_kernel[:block, :block])
    second_first = contract(piv_kernel[block:, :block], first_inverse, True)
    second_kernel = piv_kernel[block:, block:] - contract(second_first, second_first, True)
    second_inverse = inverse_factor(second_kernel)
    piv_x = lax.dynamic_slice_in_dim(x_full, rank * x_half, x_half, 1)
    piv_factor = lax.dynamic_slice_in_dim(f_full, rank * f_half, f_half, 1)
    distance, product = lax.psum(
        (
            distance_part(points, row_norms, piv_x.astype(jnp.bfloat16), square_norms(piv_x)),
            contract(prior, piv_factor, True),
        ),
        "rank",
    )
    matches = (global_ids[:, None] == pivots[None, :]).astype(jnp.float32)
    panel = jnp.exp(-distance / feature_count) + NUGGET * matches - product
    first_full = contract(panel[:, :block], first_inverse, True)
    second_panel = panel[:, block:] - contract(first_full, second_first, True)
    first_columns = lax.dynamic_slice_in_dim(first_full, col_start, col_count, 1)
    second_columns = contract(
        second_panel, lax.dynamic_slice_in_dim(second_inverse, col_start, col_count, 0), True
    )
    return (first_columns, second_columns)


def solution(mesh):
    return jax.shard_map(
        per_device,
        mesh=mesh,
        in_specs=(P("pts", "rank"), P("pts", "rank"), P(), P()),
        out_specs=(P("pts", "rank"), P("pts", "rank")),
        check_vma=False,
    )
```

```python
import jax
import jax.numpy as jnp
from jax import lax
from jax.sharding import PartitionSpec as P

NUGGET = 2.0


def contract(left_rows, right_rows, precise):
    dims = (((1,), (1,)), ((), ()))
    if precise:
        return lax.dot_general(
            left_rows,
            right_rows,
            dims,
            precision=lax.Precision.HIGHEST,
            preferred_element_type=jnp.float32,
        )
    return lax.dot_general(left_rows, right_rows, dims, preferred_element_type=jnp.float32)


def owned_rows(source, pivots, first_id):
    row_count = source.shape[0]
    local_index = pivots - first_id
    inside = (local_index >= 0) & (local_index < row_count)
    picked = jnp.take(source, jnp.clip(local_index, 0, row_count - 1), axis=0)
    return jnp.where(inside[:, None], picked.astype(jnp.float32), 0.0)


def square_norms(values):
    wide = values.astype(jnp.float32)
    return jnp.sum(wide * wide, axis=1)


def distance_part(left_rows, left_norms, right_rows, right_norms):
    return left_norms[:, None] + right_norms[None, :] - 2.0 * contract(left_rows, right_rows, False)


def inverse_factor(kernel_block):
    lower_factor = jnp.linalg.cholesky(kernel_block)
    identity = jnp.eye(kernel_block.shape[0], dtype=jnp.float32)
    return jax.scipy.linalg.solve_triangular(lower_factor, identity, lower=True)


def butterfly_sum(values, steps):
    kept = []
    for axis, bit in steps:
        size = lax.axis_size(axis)
        pairs = [(i, i ^ bit) for i in range(size)]
        upper = (lax.axis_index(axis) & bit) != 0
        half = values[0].shape[0] // 2
        mine = [jnp.where(upper, v[half:], v[:half]) for v in values]
        other = [jnp.where(upper, v[:half], v[half:]) for v in values]
        values = [m + r for m, r in zip(mine, lax.ppermute(other, axis, pairs))]
        kept.append((axis, pairs, upper))
    for axis, pairs, upper in reversed(kept):
        received = lax.ppermute(values, axis, pairs)
        values = [
            jnp.concatenate([jnp.where(upper, r, v), jnp.where(upper, v, r)])
            for v, r in zip(values, received)
        ]
    return values


def per_device(points, prior, first_pivots, second_pivots):
    row_count, x_half = points.shape
    f_half = prior.shape[1]
    first_id = lax.axis_index("pts") * row_count
    global_ids = first_id + lax.iota(jnp.int32, row_count)
    rank = lax.axis_index("rank")
    rank_count = lax.axis_size("rank")
    block = first_pivots.shape[0]
    col_count = block // rank_count
    col_start = rank * col_count
    feature_count = x_half * rank_count
    pivots = jnp.concatenate([first_pivots, second_pivots])
    row_norms = square_norms(points)
    x_slot = jnp.zeros((2 * block, feature_count), jnp.float32)
    f_slot = jnp.zeros((2 * block, f_half * rank_count), jnp.float32)
    x_slot = lax.dynamic_update_slice_in_dim(x_slot, owned_rows(points, pivots, first_id), rank * x_half, 1)
    f_slot = lax.dynamic_update_slice_in_dim(f_slot, owned_rows(prior, pivots, first_id), rank * f_half, 1)
    steps = [("rank", 1)] + [("pts", bit) for bit in (1, 8, 32, 2, 16, 64, 4)]
    x_full, f_full = butterfly_sum([x_slot, f_slot], steps)
    x_wide = x_full.astype(jnp.bfloat16)
    full_norms = square_norms(x_full)
    piv_distance = distance_part(x_wide, full_norms, x_wide, full_norms)
    identity = jnp.eye(2 * block, dtype=jnp.float32)
    piv_kernel = jnp.exp(-piv_distance / feature_count) + NUGGET * identity - contract(f_full, f_full, True)
    first_inverse = inverse_factor(piv_kernel[:block, :block])
    second_first = contract(piv_kernel[block:, :block], first_inverse, True)
    second_kernel = piv_kernel[block:, block:] - contract(second_first, second_first, True)
    second_inverse = inverse_factor(second_kernel)
    piv_x = lax.dynamic_slice_in_dim(x_full, rank * x_half, x_half, 1)
    piv_factor = lax.dynamic_slice_in_dim(f_full, rank * f_half, f_half, 1)
    distance, product = lax.psum(
        (
            distance_part(points, row_norms, piv_x.astype(jnp.bfloat16), square_norms(piv_x)),
            contract(prior, piv_factor, True),
        ),
        "rank",
    )
    matches = (global_ids[:, None] == pivots[None, :]).astype(jnp.float32)
    panel = jnp.exp(-distance / feature_count) + NUGGET * matches - product
    first_full = contract(panel[:, :block], first_inverse, True)
    second_panel = panel[:, block:] - contract(first_full, second_first, True)
    first_columns = lax.dynamic_slice_in_dim(first_full, col_start, col_count, 1)
    second_columns = contract(
        second_panel, lax.dynamic_slice_in_dim(second_inverse, col_start, col_count, 0), True
    )
    return (first_columns, second_columns)


def solution(mesh):
    return jax.shard_map(
        per_device,
        mesh=mesh,
        in_specs=(P("pts", "rank"), P("pts", "rank"), P(), P()),
        out_specs=(P("pts", "rank"), P("pts", "rank")),
        check_vma=False,
    )
```

```python
import jax
import jax.numpy as jnp
from jax import lax
from jax.sharding import PartitionSpec as P

NUGGET = 2.0


def contract(left_rows, right_rows, precise):
    dims = (((1,), (1,)), ((), ()))
    if precise:
        return lax.dot_general(
            left_rows,
            right_rows,
            dims,
            precision=lax.Precision.HIGHEST,
            preferred_element_type=jnp.float32,
        )
    return lax.dot_general(left_rows, right_rows, dims, preferred_element_type=jnp.float32)


def owned_rows(source, pivots, first_id):
    row_count = source.shape[0]
    local_index = pivots - first_id
    inside = (local_index >= 0) & (local_index < row_count)
    picked = jnp.take(source, jnp.clip(local_index, 0, row_count - 1), axis=0)
    return jnp.where(inside[:, None], picked.astype(jnp.float32), 0.0)


def square_norms(values):
    wide = values.astype(jnp.float32)
    return jnp.sum(wide * wide, axis=1)


def distance_part(left_rows, left_norms, right_rows, right_norms):
    return left_norms[:, None] + right_norms[None, :] - 2.0 * contract(left_rows, right_rows, False)


def inverse_factor(kernel_block):
    lower_factor = jnp.linalg.cholesky(kernel_block)
    identity = jnp.eye(kernel_block.shape[0], dtype=jnp.float32)
    return jax.scipy.linalg.solve_triangular(lower_factor, identity, lower=True)


def butterfly_sum(values, steps):
    kept = []
    for axis, shift, radix in steps:
        size = lax.axis_size(axis)
        digit = (lax.axis_index(axis) >> shift) % radix
        chunk = values[0].shape[0] // radix
        received = []
        for t in range(1, radix):
            pairs = [(i, i ^ (t << shift)) for i in range(size)]
            sent = [lax.dynamic_slice_in_dim(v, (digit ^ t) * chunk, chunk, 0) for v in values]
            received.append(lax.ppermute(sent, axis, pairs))
        mine = [lax.dynamic_slice_in_dim(v, digit * chunk, chunk, 0) for v in values]
        for part in received:
            mine = [m + r for m, r in zip(mine, part)]
        values = mine
        kept.append((axis, shift, radix, digit, chunk))
    for axis, shift, radix, digit, chunk in reversed(kept):
        size = lax.axis_size(axis)
        whole = [
            lax.dynamic_update_slice_in_dim(
                jnp.zeros((radix * chunk,) + v.shape[1:], v.dtype), v, digit * chunk, 0
            )
            for v in values
        ]
        for t in range(1, radix):
            pairs = [(i, i ^ (t << shift)) for i in range(size)]
            part = lax.ppermute(values, axis, pairs)
            whole = [
                lax.dynamic_update_slice_in_dim(w, r, (digit ^ t) * chunk, 0)
                for w, r in zip(whole, part)
            ]
        values = whole
    return values


def per_device(points, prior, first_pivots, second_pivots):
    row_count, x_half = points.shape
    f_half = prior.shape[1]
    first_id = lax.axis_index("pts") * row_count
    global_ids = first_id + lax.iota(jnp.int32, row_count)
    rank = lax.axis_index("rank")
    rank_count = lax.axis_size("rank")
    block = first_pivots.shape[0]
    col_count = block // rank_count
    col_start = rank * col_count
    feature_count = x_half * rank_count
    pivots = jnp.concatenate([first_pivots, second_pivots])
    row_norms = square_norms(points)
    x_slot = jnp.zeros((2 * block, feature_count), jnp.float32)
    f_slot = jnp.zeros((2 * block, f_half * rank_count), jnp.float32)
    x_slot = lax.dynamic_update_slice_in_dim(x_slot, owned_rows(points, pivots, first_id), rank * x_half, 1)
    f_slot = lax.dynamic_update_slice_in_dim(f_slot, owned_rows(prior, pivots, first_id), rank * f_half, 1)
    steps = [("rank", 0, 2), ("pts", 3, 4), ("pts", 5, 4), ("pts", 0, 8)]
    (rows_full,) = butterfly_sum([jnp.concatenate([x_slot, f_slot], axis=1)], steps)
    x_full = rows_full[:, :feature_count]
    f_full = rows_full[:, feature_count:]
    x_wide = x_full.astype(jnp.bfloat16)
    full_norms = square_norms(x_full)
    piv_distance = distance_part(x_wide, full_norms, x_wide, full_norms)
    identity = jnp.eye(2 * block, dtype=jnp.float32)
    piv_kernel = jnp.exp(-piv_distance / feature_count) + NUGGET * identity - contract(f_full, f_full, True)
    first_inverse = inverse_factor(piv_kernel[:block, :block])
    second_first = contract(piv_kernel[block:, :block], first_inverse, True)
    second_kernel = piv_kernel[block:, block:] - contract(second_first, second_first, True)
    second_inverse = inverse_factor(second_kernel)
    piv_x = lax.dynamic_slice_in_dim(x_full, rank * x_half, x_half, 1)
    piv_factor = lax.dynamic_slice_in_dim(f_full, rank * f_half, f_half, 1)
    distance, product = lax.psum(
        (
            distance_part(points, row_norms, piv_x.astype(jnp.bfloat16), square_norms(piv_x)),
            contract(prior, piv_factor, True),
        ),
        "rank",
    )
    matches = (global_ids[:, None] == pivots[None, :]).astype(jnp.float32)
    panel = jnp.exp(-distance / feature_count) + NUGGET * matches - product
    first_full = contract(panel[:, :block], first_inverse, True)
    second_panel = panel[:, block:] - contract(first_full, second_first, True)
    first_columns = lax.dynamic_slice_in_dim(first_full, col_start, col_count, 1)
    second_columns = contract(
        second_panel, lax.dynamic_slice_in_dim(second_inverse, col_start, col_count, 0), True
    )
    return (first_columns, second_columns)


def solution(mesh):
    return jax.shard_map(
        per_device,
        mesh=mesh,
        in_specs=(P("pts", "rank"), P("pts", "rank"), P(), P()),
        out_specs=(P("pts", "rank"), P("pts", "rank")),
        check_vma=False,
    )
```

```python
import jax
import jax.numpy as jnp
from jax import lax
from jax.sharding import PartitionSpec as P

NUGGET = 2.0


def contract(left_rows, right_rows, precise):
    dims = (((1,), (1,)), ((), ()))
    if precise:
        return lax.dot_general(
            left_rows,
            right_rows,
            dims,
            precision=lax.Precision.HIGHEST,
            preferred_element_type=jnp.float32,
        )
    return lax.dot_general(left_rows, right_rows, dims, preferred_element_type=jnp.float32)


def owned_rows(source, pivots, first_id):
    row_count = source.shape[0]
    local_index = pivots - first_id
    inside = (local_index >= 0) & (local_index < row_count)
    picked = jnp.take(source, jnp.clip(local_index, 0, row_count - 1), axis=0)
    return jnp.where(inside[:, None], picked.astype(jnp.float32), 0.0)


def square_norms(values):
    wide = values.astype(jnp.float32)
    return jnp.sum(wide * wide, axis=1)


def distance_part(left_rows, left_norms, right_rows, right_norms):
    return left_norms[:, None] + right_norms[None, :] - 2.0 * contract(left_rows, right_rows, False)


def inverse_factor(kernel_block):
    size = kernel_block.shape[0]
    half = size // 2
    identity = jnp.eye(half, dtype=jnp.float32)
    upper_factor = jnp.linalg.cholesky(kernel_block[:half, :half])
    upper_inverse = jax.scipy.linalg.solve_triangular(upper_factor, identity, lower=True)
    cross_factor = contract(kernel_block[half:, :half], upper_inverse, True)
    rest = kernel_block[half:, half:] - contract(cross_factor, cross_factor, True)
    lower_factor = jnp.linalg.cholesky(rest)
    lower_inverse = jax.scipy.linalg.solve_triangular(lower_factor, identity, lower=True)
    cross_inverse = -lax.dot_general(
        lower_inverse,
        contract(cross_factor, upper_inverse.T, True),
        (((1,), (0,)), ((), ())),
        precision=lax.Precision.HIGHEST,
        preferred_element_type=jnp.float32,
    )
    zeros = jnp.zeros((half, size - half), jnp.float32)
    return jnp.concatenate(
        [
            jnp.concatenate([upper_inverse, zeros], axis=1),
            jnp.concatenate([cross_inverse, lower_inverse], axis=1),
        ],
        axis=0,
    )


def butterfly_sum(values, steps):
    kept = []
    for axis, shift, radix in steps:
        size = lax.axis_size(axis)
        digit = (lax.axis_index(axis) >> shift) % radix
        chunk = values[0].shape[0] // radix
        received = []
        for t in range(1, radix):
            pairs = [(i, i ^ (t << shift)) for i in range(size)]
            sent = [lax.dynamic_slice_in_dim(v, (digit ^ t) * chunk, chunk, 0) for v in values]
            received.append(lax.ppermute(sent, axis, pairs))
        mine = [lax.dynamic_slice_in_dim(v, digit * chunk, chunk, 0) for v in values]
        for part in received:
            mine = [m + r for m, r in zip(mine, part)]
        values = mine
        kept.append((axis, shift, radix, digit, chunk))
    for axis, shift, radix, digit, chunk in reversed(kept):
        size = lax.axis_size(axis)
        whole = [
            lax.dynamic_update_slice_in_dim(
                jnp.zeros((radix * chunk,) + v.shape[1:], v.dtype), v, digit * chunk, 0
            )
            for v in values
        ]
        for t in range(1, radix):
            pairs = [(i, i ^ (t << shift)) for i in range(size)]
            part = lax.ppermute(values, axis, pairs)
            whole = [
                lax.dynamic_update_slice_in_dim(w, r, (digit ^ t) * chunk, 0)
                for w, r in zip(whole, part)
            ]
        values = whole
    return values


def per_device(points, prior, first_pivots, second_pivots):
    row_count, x_half = points.shape
    f_half = prior.shape[1]
    first_id = lax.axis_index("pts") * row_count
    global_ids = first_id + lax.iota(jnp.int32, row_count)
    rank = lax.axis_index("rank")
    rank_count = lax.axis_size("rank")
    block = first_pivots.shape[0]
    col_count = block // rank_count
    col_start = rank * col_count
    feature_count = x_half * rank_count
    pivots = jnp.concatenate([first_pivots, second_pivots])
    row_norms = square_norms(points)
    x_slot = jnp.zeros((2 * block, feature_count), jnp.float32)
    f_slot = jnp.zeros((2 * block, f_half * rank_count), jnp.float32)
    x_slot = lax.dynamic_update_slice_in_dim(x_slot, owned_rows(points, pivots, first_id), rank * x_half, 1)
    f_slot = lax.dynamic_update_slice_in_dim(f_slot, owned_rows(prior, pivots, first_id), rank * f_half, 1)
    steps = [("rank", 0, 2), ("pts", 3, 4), ("pts", 5, 4), ("pts", 0, 8)]
    (rows_full,) = butterfly_sum([jnp.concatenate([x_slot, f_slot], axis=1)], steps)
    x_full = rows_full[:, :feature_count]
    f_full = rows_full[:, feature_count:]
    x_wide = x_full.astype(jnp.bfloat16)
    full_norms = square_norms(x_full)
    piv_distance = distance_part(x_wide, full_norms, x_wide, full_norms)
    identity = jnp.eye(2 * block, dtype=jnp.float32)
    piv_kernel = jnp.exp(-piv_distance / feature_count) + NUGGET * identity - contract(f_full, f_full, True)
    first_inverse = inverse_factor(piv_kernel[:block, :block])
    second_first = contract(piv_kernel[block:, :block], first_inverse, True)
    second_kernel = piv_kernel[block:, block:] - contract(second_first, second_first, True)
    second_inverse = inverse_factor(second_kernel)
    piv_x = lax.dynamic_slice_in_dim(x_full, rank * x_half, x_half, 1)
    piv_factor = lax.dynamic_slice_in_dim(f_full, rank * f_half, f_half, 1)
    distance, product = lax.psum(
        (
            distance_part(points, row_norms, piv_x.astype(jnp.bfloat16), square_norms(piv_x)),
            contract(prior, piv_factor, True),
        ),
        "rank",
    )
    matches = (global_ids[:, None] == pivots[None, :]).astype(jnp.float32)
    panel = jnp.exp(-distance / feature_count) + NUGGET * matches - product
    first_full = contract(panel[:, :block], first_inverse, True)
    second_panel = panel[:, block:] - contract(first_full, second_first, True)
    first_columns = lax.dynamic_slice_in_dim(first_full, col_start, col_count, 1)
    second_columns = contract(
        second_panel, lax.dynamic_slice_in_dim(second_inverse, col_start, col_count, 0), True
    )
    return (first_columns, second_columns)


def solution(mesh):
    return jax.shard_map(
        per_device,
        mesh=mesh,
        in_specs=(P("pts", "rank"), P("pts", "rank"), P(), P()),
        out_specs=(P("pts", "rank"), P("pts", "rank")),
        check_vma=False,
    )
```

```python
import jax
import jax.numpy as jnp
from jax import lax
from jax.sharding import PartitionSpec as P

NUGGET = 2.0


def contract(left_rows, right_rows, precise):
    dims = (((1,), (1,)), ((), ()))
    if precise:
        return lax.dot_general(
            left_rows,
            right_rows,
            dims,
            precision=lax.Precision.HIGHEST,
            preferred_element_type=jnp.float32,
        )
    return lax.dot_general(left_rows, right_rows, dims, preferred_element_type=jnp.float32)


def owned_rows(source, pivots, first_id):
    row_count = source.shape[0]
    local_index = pivots - first_id
    inside = (local_index >= 0) & (local_index < row_count)
    picked = jnp.take(source, jnp.clip(local_index, 0, row_count - 1), axis=0)
    return jnp.where(inside[:, None], picked.astype(jnp.float32), 0.0)


def square_norms(values):
    wide = values.astype(jnp.float32)
    return jnp.sum(wide * wide, axis=1)


def distance_part(left_rows, left_norms, right_rows, right_norms):
    return left_norms[:, None] + right_norms[None, :] - 2.0 * contract(left_rows, right_rows, False)


def inverse_factor(kernel_block):
    size = kernel_block.shape[0]
    half = size // 2
    identity = jnp.eye(half, dtype=jnp.float32)
    upper_factor = jnp.linalg.cholesky(kernel_block[:half, :half])
    upper_inverse = jax.scipy.linalg.solve_triangular(upper_factor, identity, lower=True)
    cross_factor = contract(kernel_block[half:, :half], upper_inverse, True)
    rest = kernel_block[half:, half:] - contract(cross_factor, cross_factor, True)
    lower_factor = jnp.linalg.cholesky(rest)
    lower_inverse = jax.scipy.linalg.solve_triangular(lower_factor, identity, lower=True)
    cross_inverse = -lax.dot_general(
        lower_inverse,
        contract(cross_factor, upper_inverse.T, True),
        (((1,), (0,)), ((), ())),
        precision=lax.Precision.HIGHEST,
        preferred_element_type=jnp.float32,
    )
    zeros = jnp.zeros((half, size - half), jnp.float32)
    return jnp.concatenate(
        [
            jnp.concatenate([upper_inverse, zeros], axis=1),
            jnp.concatenate([cross_inverse, lower_inverse], axis=1),
        ],
        axis=0,
    )


def butterfly_sum(values, steps):
    kept = []
    for axis, shift, radix in steps:
        size = lax.axis_size(axis)
        digit = (lax.axis_index(axis) >> shift) % radix
        chunk = values[0].shape[0] // radix
        received = []
        for t in range(1, radix):
            pairs = [(i, i ^ (t << shift)) for i in range(size)]
            sent = [lax.dynamic_slice_in_dim(v, (digit ^ t) * chunk, chunk, 0) for v in values]
            received.append(lax.ppermute(sent, axis, pairs))
        mine = [lax.dynamic_slice_in_dim(v, digit * chunk, chunk, 0) for v in values]
        for part in received:
            mine = [m + r for m, r in zip(mine, part)]
        values = mine
        kept.append((axis, shift, radix, digit, chunk))
    for axis, shift, radix, digit, chunk in reversed(kept):
        size = lax.axis_size(axis)
        whole = [
            lax.dynamic_update_slice_in_dim(
                jnp.zeros((radix * chunk,) + v.shape[1:], v.dtype), v, digit * chunk, 0
            )
            for v in values
        ]
        for t in range(1, radix):
            pairs = [(i, i ^ (t << shift)) for i in range(size)]
            part = lax.ppermute(values, axis, pairs)
            whole = [
                lax.dynamic_update_slice_in_dim(w, r, (digit ^ t) * chunk, 0)
                for w, r in zip(whole, part)
            ]
        values = whole
    return values


def per_device(points, prior, first_pivots, second_pivots):
    row_count, x_half = points.shape
    f_half = prior.shape[1]
    first_id = lax.axis_index("pts") * row_count
    global_ids = first_id + lax.iota(jnp.int32, row_count)
    rank = lax.axis_index("rank")
    rank_count = lax.axis_size("rank")
    block = first_pivots.shape[0]
    col_count = block // rank_count
    col_start = rank * col_count
    feature_count = x_half * rank_count
    pivots = jnp.concatenate([first_pivots, second_pivots])
    row_norms = square_norms(points)
    steps = [("rank", 0, 2), ("pts", 3, 4), ("pts", 5, 4), ("pts", 0, 8)]

    def whole_rows(block_pivots, after):
        x_slot = jnp.zeros((block, feature_count), jnp.float32)
        f_slot = jnp.zeros((block, f_half * rank_count), jnp.float32)
        x_slot = lax.dynamic_update_slice_in_dim(
            x_slot, owned_rows(points, block_pivots, first_id), rank * x_half, 1
        )
        f_slot = lax.dynamic_update_slice_in_dim(
            f_slot, owned_rows(prior, block_pivots, first_id), rank * f_half, 1
        )
        slots = jnp.concatenate([x_slot, f_slot], axis=1)
        if after is not None:
            slots = slots + jnp.zeros_like(slots) * after[0, 0]
        (rows,) = butterfly_sum([slots], steps)
        return rows

    def block_kernel(left, right):
        left_x, right_x = left[:, :feature_count], right[:, :feature_count]
        distance = distance_part(
            left_x.astype(jnp.bfloat16), square_norms(left_x), right_x.astype(jnp.bfloat16), square_norms(right_x)
        )
        product = contract(left[:, feature_count:], right[:, feature_count:], True)
        return jnp.exp(-distance / feature_count) - product

    identity = jnp.eye(block, dtype=jnp.float32)
    first_rows = whole_rows(first_pivots, None)
    second_rows = whole_rows(second_pivots, first_rows)
    first_inverse = inverse_factor(block_kernel(first_rows, first_rows) + NUGGET * identity)
    second_first = contract(block_kernel(second_rows, first_rows), first_inverse, True)
    second_kernel = (
        block_kernel(second_rows, second_rows) + NUGGET * identity - contract(second_first, second_first, True)
    )
    second_inverse = inverse_factor(second_kernel)
    x_full = jnp.concatenate([first_rows[:, :feature_count], second_rows[:, :feature_count]])
    f_full = jnp.concatenate([first_rows[:, feature_count:], second_rows[:, feature_count:]])
    piv_x = lax.dynamic_slice_in_dim(x_full, rank * x_half, x_half, 1)
    piv_factor = lax.dynamic_slice_in_dim(f_full, rank * f_half, f_half, 1)
    distance, product = lax.psum(
        (
            distance_part(points, row_norms, piv_x.astype(jnp.bfloat16), square_norms(piv_x)),
            contract(prior, piv_factor, True),
        ),
        "rank",
    )
    matches = (global_ids[:, None] == pivots[None, :]).astype(jnp.float32)
    panel = jnp.exp(-distance / feature_count) + NUGGET * matches - product
    first_full = contract(panel[:, :block], first_inverse, True)
    second_panel = panel[:, block:] - contract(first_full, second_first, True)
    first_columns = lax.dynamic_slice_in_dim(first_full, col_start, col_count, 1)
    second_columns = contract(
        second_panel, lax.dynamic_slice_in_dim(second_inverse, col_start, col_count, 0), True
    )
    return (first_columns, second_columns)


def solution(mesh):
    return jax.shard_map(
        per_device,
        mesh=mesh,
        in_specs=(P("pts", "rank"), P("pts", "rank"), P(), P()),
        out_specs=(P("pts", "rank"), P("pts", "rank")),
        check_vma=False,
    )
```

```python
import jax
import jax.numpy as jnp
from jax import lax
from jax.sharding import PartitionSpec as P

NUGGET = 2.0


def contract(left_rows, right_rows, precise):
    dims = (((1,), (1,)), ((), ()))
    if precise:
        return lax.dot_general(
            left_rows,
            right_rows,
            dims,
            precision=lax.Precision.HIGHEST,
            preferred_element_type=jnp.float32,
        )
    return lax.dot_general(left_rows, right_rows, dims, preferred_element_type=jnp.float32)


def owned_rows(source, pivots, first_id):
    row_count = source.shape[0]
    local_index = pivots - first_id
    inside = (local_index >= 0) & (local_index < row_count)
    picked = jnp.take(source, jnp.clip(local_index, 0, row_count - 1), axis=0)
    return jnp.where(inside[:, None], picked.astype(jnp.float32), 0.0)


def square_norms(values):
    wide = values.astype(jnp.float32)
    return jnp.sum(wide * wide, axis=1)


def distance_part(left_rows, left_norms, right_rows, right_norms):
    return left_norms[:, None] + right_norms[None, :] - 2.0 * contract(left_rows, right_rows, False)


def inverse_factor(kernel_block):
    size = kernel_block.shape[0]
    half = size // 2
    identity = jnp.eye(half, dtype=jnp.float32)
    upper_factor = jnp.linalg.cholesky(kernel_block[:half, :half])
    upper_inverse = jax.scipy.linalg.solve_triangular(upper_factor, identity, lower=True)
    cross_factor = contract(kernel_block[half:, :half], upper_inverse, True)
    rest = kernel_block[half:, half:] - contract(cross_factor, cross_factor, True)
    lower_factor = jnp.linalg.cholesky(rest)
    lower_inverse = jax.scipy.linalg.solve_triangular(lower_factor, identity, lower=True)
    cross_inverse = -lax.dot_general(
        lower_inverse,
        contract(cross_factor, upper_inverse.T, True),
        (((1,), (0,)), ((), ())),
        precision=lax.Precision.HIGHEST,
        preferred_element_type=jnp.float32,
    )
    zeros = jnp.zeros((half, size - half), jnp.float32)
    return jnp.concatenate(
        [
            jnp.concatenate([upper_inverse, zeros], axis=1),
            jnp.concatenate([cross_inverse, lower_inverse], axis=1),
        ],
        axis=0,
    )


def butterfly_sum(values, steps):
    kept = []
    for axis, shift, radix in steps:
        size = lax.axis_size(axis)
        digit = (lax.axis_index(axis) >> shift) % radix
        chunk = values[0].shape[0] // radix
        received = []
        for t in range(1, radix):
            pairs = [(i, i ^ (t << shift)) for i in range(size)]
            sent = [lax.dynamic_slice_in_dim(v, (digit ^ t) * chunk, chunk, 0) for v in values]
            received.append(lax.ppermute(sent, axis, pairs))
        mine = [lax.dynamic_slice_in_dim(v, digit * chunk, chunk, 0) for v in values]
        for part in received:
            mine = [m + r for m, r in zip(mine, part)]
        values = mine
        kept.append((axis, shift, radix, digit, chunk))
    for axis, shift, radix, digit, chunk in reversed(kept):
        size = lax.axis_size(axis)
        whole = [
            lax.dynamic_update_slice_in_dim(
                jnp.zeros((radix * chunk,) + v.shape[1:], v.dtype), v, digit * chunk, 0
            )
            for v in values
        ]
        for t in range(1, radix):
            pairs = [(i, i ^ (t << shift)) for i in range(size)]
            part = lax.ppermute(values, axis, pairs)
            whole = [
                lax.dynamic_update_slice_in_dim(w, r, (digit ^ t) * chunk, 0)
                for w, r in zip(whole, part)
            ]
        values = whole
    return values


def per_device(points, prior, first_pivots, second_pivots):
    row_count, x_half = points.shape
    f_half = prior.shape[1]
    first_id = lax.axis_index("pts") * row_count
    global_ids = first_id + lax.iota(jnp.int32, row_count)
    rank = lax.axis_index("rank")
    rank_count = lax.axis_size("rank")
    block = first_pivots.shape[0]
    col_count = block // rank_count
    col_start = rank * col_count
    feature_count = x_half * rank_count
    pivots = jnp.concatenate([first_pivots, second_pivots])
    row_norms = square_norms(points)
    x_slot = jnp.zeros((2 * block, feature_count), jnp.float32)
    f_slot = jnp.zeros((2 * block, f_half * rank_count), jnp.float32)
    x_slot = lax.dynamic_update_slice_in_dim(x_slot, owned_rows(points, pivots, first_id), rank * x_half, 1)
    f_slot = lax.dynamic_update_slice_in_dim(f_slot, owned_rows(prior, pivots, first_id), rank * f_half, 1)
    steps = [("rank", 0, 2), ("pts", 3, 4), ("pts", 5, 4), ("pts", 0, 4), ("pts", 2, 2)]
    (rows_full,) = butterfly_sum([jnp.concatenate([x_slot, f_slot], axis=1)], steps)
    x_full = rows_full[:, :feature_count]
    f_full = rows_full[:, feature_count:]
    x_wide = x_full.astype(jnp.bfloat16)
    full_norms = square_norms(x_full)
    piv_distance = distance_part(x_wide, full_norms, x_wide, full_norms)
    identity = jnp.eye(2 * block, dtype=jnp.float32)
    piv_kernel = jnp.exp(-piv_distance / feature_count) + NUGGET * identity - contract(f_full, f_full, True)
    first_inverse = inverse_factor(piv_kernel[:block, :block])
    second_first = contract(piv_kernel[block:, :block], first_inverse, True)
    second_kernel = piv_kernel[block:, block:] - contract(second_first, second_first, True)
    second_inverse = inverse_factor(second_kernel)
    piv_x = lax.dynamic_slice_in_dim(x_full, rank * x_half, x_half, 1)
    piv_factor = lax.dynamic_slice_in_dim(f_full, rank * f_half, f_half, 1)
    distance, product = lax.psum(
        (
            distance_part(points, row_norms, piv_x.astype(jnp.bfloat16), square_norms(piv_x)),
            contract(prior, piv_factor, True),
        ),
        "rank",
    )
    matches = (global_ids[:, None] == pivots[None, :]).astype(jnp.float32)
    panel = jnp.exp(-distance / feature_count) + NUGGET * matches - product
    first_full = contract(panel[:, :block], first_inverse, True)
    second_panel = panel[:, block:] - contract(first_full, second_first, True)
    first_columns = lax.dynamic_slice_in_dim(first_full, col_start, col_count, 1)
    second_columns = contract(
        second_panel, lax.dynamic_slice_in_dim(second_inverse, col_start, col_count, 0), True
    )
    return (first_columns, second_columns)


def solution(mesh):
    return jax.shard_map(
        per_device,
        mesh=mesh,
        in_specs=(P("pts", "rank"), P("pts", "rank"), P(), P()),
        out_specs=(P("pts", "rank"), P("pts", "rank")),
        check_vma=False,
    )
```

```python
import jax
import jax.numpy as jnp
from jax import lax
from jax.sharding import PartitionSpec as P

NUGGET = 2.0


def contract(left_rows, right_rows, precise):
    dims = (((1,), (1,)), ((), ()))
    if precise:
        return lax.dot_general(
            left_rows,
            right_rows,
            dims,
            precision=lax.Precision.HIGHEST,
            preferred_element_type=jnp.float32,
        )
    return lax.dot_general(left_rows, right_rows, dims, preferred_element_type=jnp.float32)


def owned_rows(source, pivots, first_id):
    row_count = source.shape[0]
    local_index = pivots - first_id
    inside = (local_index >= 0) & (local_index < row_count)
    picked = jnp.take(source, jnp.clip(local_index, 0, row_count - 1), axis=0)
    return jnp.where(inside[:, None], picked.astype(jnp.float32), 0.0)


def square_norms(values):
    wide = values.astype(jnp.float32)
    return jnp.sum(wide * wide, axis=1)


def distance_part(left_rows, left_norms, right_rows, right_norms):
    return left_norms[:, None] + right_norms[None, :] - 2.0 * contract(left_rows, right_rows, False)


def inverse_factor(kernel_block):
    size = kernel_block.shape[0]
    half = size // 2
    identity = jnp.eye(half, dtype=jnp.float32)
    upper_factor = jnp.linalg.cholesky(kernel_block[:half, :half])
    upper_inverse = jax.scipy.linalg.solve_triangular(upper_factor, identity, lower=True)
    cross_factor = contract(kernel_block[half:, :half], upper_inverse, True)
    rest = kernel_block[half:, half:] - contract(cross_factor, cross_factor, True)
    lower_factor = jnp.linalg.cholesky(rest)
    lower_inverse = jax.scipy.linalg.solve_triangular(lower_factor, identity, lower=True)
    cross_inverse = -lax.dot_general(
        lower_inverse,
        contract(cross_factor, upper_inverse.T, True),
        (((1,), (0,)), ((), ())),
        precision=lax.Precision.HIGHEST,
        preferred_element_type=jnp.float32,
    )
    zeros = jnp.zeros((half, size - half), jnp.float32)
    return jnp.concatenate(
        [
            jnp.concatenate([upper_inverse, zeros], axis=1),
            jnp.concatenate([cross_inverse, lower_inverse], axis=1),
        ],
        axis=0,
    )


def butterfly_sum(values, steps):
    kept = []
    for axis, shift, radix in steps:
        size = lax.axis_size(axis)
        digit = (lax.axis_index(axis) >> shift) % radix
        chunk = values[0].shape[0] // radix
        received = []
        for t in range(1, radix):
            pairs = [(i, i ^ (t << shift)) for i in range(size)]
            sent = [lax.dynamic_slice_in_dim(v, (digit ^ t) * chunk, chunk, 0) for v in values]
            received.append(lax.ppermute(sent, axis, pairs))
        mine = [lax.dynamic_slice_in_dim(v, digit * chunk, chunk, 0) for v in values]
        for part in received:
            mine = [m + r for m, r in zip(mine, part)]
        values = mine
        kept.append((axis, shift, radix, digit, chunk))
    for axis, shift, radix, digit, chunk in reversed(kept):
        size = lax.axis_size(axis)
        whole = [
            lax.dynamic_update_slice_in_dim(
                jnp.zeros((radix * chunk,) + v.shape[1:], v.dtype), v, digit * chunk, 0
            )
            for v in values
        ]
        for t in range(1, radix):
            pairs = [(i, i ^ (t << shift)) for i in range(size)]
            part = lax.ppermute(values, axis, pairs)
            whole = [
                lax.dynamic_update_slice_in_dim(w, r, (digit ^ t) * chunk, 0)
                for w, r in zip(whole, part)
            ]
        values = whole
    return values


def per_device(points, prior, first_pivots, second_pivots):
    row_count, x_half = points.shape
    f_half = prior.shape[1]
    first_id = lax.axis_index("pts") * row_count
    global_ids = first_id + lax.iota(jnp.int32, row_count)
    rank = lax.axis_index("rank")
    rank_count = lax.axis_size("rank")
    block = first_pivots.shape[0]
    col_count = block // rank_count
    col_start = rank * col_count
    feature_count = x_half * rank_count
    pivots = jnp.concatenate([first_pivots, second_pivots])
    row_norms = square_norms(points)
    select = pivots[:, None] == global_ids[None, :]
    take = (((1,), (0,)), ((), ()))
    x_rows = lax.dot_general(
        select.astype(points.dtype), points, take, preferred_element_type=jnp.float32
    )
    f_rows = lax.dot_general(
        select.astype(jnp.float32),
        prior,
        take,
        precision=lax.Precision.HIGHEST,
        preferred_element_type=jnp.float32,
    )
    x_slot = jnp.zeros((2 * block, feature_count), jnp.float32)
    f_slot = jnp.zeros((2 * block, f_half * rank_count), jnp.float32)
    x_slot = lax.dynamic_update_slice_in_dim(x_slot, x_rows, rank * x_half, 1)
    f_slot = lax.dynamic_update_slice_in_dim(f_slot, f_rows, rank * f_half, 1)
    steps = [("rank", 0, 2), ("pts", 3, 4), ("pts", 5, 4), ("pts", 0, 4), ("pts", 2, 2)]
    (rows_full,) = butterfly_sum([jnp.concatenate([x_slot, f_slot], axis=1)], steps)
    x_full = rows_full[:, :feature_count]
    f_full = rows_full[:, feature_count:]
    x_wide = x_full.astype(jnp.bfloat16)
    full_norms = square_norms(x_full)
    piv_distance = distance_part(x_wide, full_norms, x_wide, full_norms)
    identity = jnp.eye(2 * block, dtype=jnp.float32)
    piv_kernel = jnp.exp(-piv_distance / feature_count) + NUGGET * identity - contract(f_full, f_full, True)
    first_inverse = inverse_factor(piv_kernel[:block, :block])
    second_first = contract(piv_kernel[block:, :block], first_inverse, True)
    second_kernel = piv_kernel[block:, block:] - contract(second_first, second_first, True)
    second_inverse = inverse_factor(second_kernel)
    piv_x = lax.dynamic_slice_in_dim(x_full, rank * x_half, x_half, 1)
    piv_factor = lax.dynamic_slice_in_dim(f_full, rank * f_half, f_half, 1)
    distance, product = lax.psum(
        (
            distance_part(points, row_norms, piv_x.astype(jnp.bfloat16), square_norms(piv_x)),
            contract(prior, piv_factor, True),
        ),
        "rank",
    )
    matches = (global_ids[:, None] == pivots[None, :]).astype(jnp.float32)
    panel = jnp.exp(-distance / feature_count) + NUGGET * matches - product
    first_full = contract(panel[:, :block], first_inverse, True)
    second_panel = panel[:, block:] - contract(first_full, second_first, True)
    first_columns = lax.dynamic_slice_in_dim(first_full, col_start, col_count, 1)
    second_columns = contract(
        second_panel, lax.dynamic_slice_in_dim(second_inverse, col_start, col_count, 0), True
    )
    return (first_columns, second_columns)


def solution(mesh):
    return jax.shard_map(
        per_device,
        mesh=mesh,
        in_specs=(P("pts", "rank"), P("pts", "rank"), P(), P()),
        out_specs=(P("pts", "rank"), P("pts", "rank")),
        check_vma=False,
    )
```

```python
import jax
import jax.numpy as jnp
from jax import lax
from jax.sharding import PartitionSpec as P

NUGGET = 2.0


def contract(left_rows, right_rows, precise):
    dims = (((1,), (1,)), ((), ()))
    if precise:
        return lax.dot_general(
            left_rows,
            right_rows,
            dims,
            precision=lax.Precision.HIGHEST,
            preferred_element_type=jnp.float32,
        )
    return lax.dot_general(left_rows, right_rows, dims, preferred_element_type=jnp.float32)


def owned_rows(source, pivots, first_id):
    row_count = source.shape[0]
    local_index = pivots - first_id
    inside = (local_index >= 0) & (local_index < row_count)
    picked = jnp.take(source, jnp.clip(local_index, 0, row_count - 1), axis=0)
    return jnp.where(inside[:, None], picked.astype(jnp.float32), 0.0)


def square_norms(values):
    wide = values.astype(jnp.float32)
    return jnp.sum(wide * wide, axis=1)


def distance_part(left_rows, left_norms, right_rows, right_norms):
    return left_norms[:, None] + right_norms[None, :] - 2.0 * contract(left_rows, right_rows, False)


def inverse_factor(kernel_block):
    size = kernel_block.shape[0]
    half = size // 2
    identity = jnp.eye(half, dtype=jnp.float32)
    upper_factor = jnp.linalg.cholesky(kernel_block[:half, :half])
    upper_inverse = jax.scipy.linalg.solve_triangular(upper_factor, identity, lower=True)
    cross_factor = contract(kernel_block[half:, :half], upper_inverse, True)
    rest = kernel_block[half:, half:] - contract(cross_factor, cross_factor, True)
    lower_factor = jnp.linalg.cholesky(rest)
    lower_inverse = jax.scipy.linalg.solve_triangular(lower_factor, identity, lower=True)
    cross_inverse = -lax.dot_general(
        lower_inverse,
        contract(cross_factor, upper_inverse.T, True),
        (((1,), (0,)), ((), ())),
        precision=lax.Precision.HIGHEST,
        preferred_element_type=jnp.float32,
    )
    zeros = jnp.zeros((half, size - half), jnp.float32)
    return jnp.concatenate(
        [
            jnp.concatenate([upper_inverse, zeros], axis=1),
            jnp.concatenate([cross_inverse, lower_inverse], axis=1),
        ],
        axis=0,
    )


def butterfly_sum(values, steps):
    kept = []
    for axis, shift, radix in steps:
        size = lax.axis_size(axis)
        digit = (lax.axis_index(axis) >> shift) % radix
        chunk = values[0].shape[0] // radix
        received = []
        for t in range(1, radix):
            pairs = [(i, i ^ (t << shift)) for i in range(size)]
            sent = [lax.dynamic_slice_in_dim(v, (digit ^ t) * chunk, chunk, 0) for v in values]
            received.append(lax.ppermute(sent, axis, pairs))
        mine = [lax.dynamic_slice_in_dim(v, digit * chunk, chunk, 0) for v in values]
        for part in received:
            mine = [m + r for m, r in zip(mine, part)]
        values = mine
        kept.append((axis, shift, radix, digit, chunk))
    for axis, shift, radix, digit, chunk in reversed(kept):
        size = lax.axis_size(axis)
        whole = [
            lax.dynamic_update_slice_in_dim(
                jnp.zeros((radix * chunk,) + v.shape[1:], v.dtype), v, digit * chunk, 0
            )
            for v in values
        ]
        for t in range(1, radix):
            pairs = [(i, i ^ (t << shift)) for i in range(size)]
            part = lax.ppermute(values, axis, pairs)
            whole = [
                lax.dynamic_update_slice_in_dim(w, r, (digit ^ t) * chunk, 0)
                for w, r in zip(whole, part)
            ]
        values = whole
    return values


def per_device(points, prior, first_pivots, second_pivots):
    row_count, x_half = points.shape
    f_half = prior.shape[1]
    first_id = lax.axis_index("pts") * row_count
    global_ids = first_id + lax.iota(jnp.int32, row_count)
    rank = lax.axis_index("rank")
    rank_count = lax.axis_size("rank")
    block = first_pivots.shape[0]
    col_count = block // rank_count
    col_start = rank * col_count
    feature_count = x_half * rank_count
    pivots = jnp.concatenate([first_pivots, second_pivots])
    row_norms = square_norms(points)
    select = pivots[:, None] == global_ids[None, :]
    take = (((1,), (0,)), ((), ()))
    x_rows = lax.dot_general(
        select.astype(points.dtype), points, take, preferred_element_type=jnp.float32
    )
    f_rows = lax.dot_general(
        select.astype(jnp.float32),
        prior,
        take,
        precision=lax.Precision.HIGHEST,
        preferred_element_type=jnp.float32,
    )
    x_slot = jnp.zeros((2 * block, feature_count), jnp.float32)
    f_slot = jnp.zeros((2 * block, f_half * rank_count), jnp.float32)
    x_slot = lax.dynamic_update_slice_in_dim(x_slot, x_rows, rank * x_half, 1)
    f_slot = lax.dynamic_update_slice_in_dim(f_slot, f_rows, rank * f_half, 1)
    steps = [("rank", 0, 2), ("pts", 3, 4), ("pts", 5, 4), ("pts", 0, 4), ("pts", 2, 2)]
    (rows_full,) = butterfly_sum([jnp.concatenate([x_slot, f_slot], axis=1)], steps)
    x_full = rows_full[:, :feature_count]
    f_full = rows_full[:, feature_count:]
    x_wide = x_full.astype(jnp.bfloat16)
    full_norms = square_norms(x_full)
    piv_distance = distance_part(x_wide, full_norms, x_wide, full_norms)
    identity = jnp.eye(2 * block, dtype=jnp.float32)
    piv_kernel = jnp.exp(-piv_distance / feature_count) + NUGGET * identity - contract(f_full, f_full, True)
    first_inverse = inverse_factor(piv_kernel[:block, :block])
    second_first = contract(piv_kernel[block:, :block], first_inverse, True)
    second_kernel = piv_kernel[block:, block:] - contract(second_first, second_first, True)
    second_inverse = inverse_factor(second_kernel)
    piv_x = lax.dynamic_slice_in_dim(x_full, rank * x_half, x_half, 1)
    piv_factor = lax.dynamic_slice_in_dim(f_full, rank * f_half, f_half, 1)
    partials = (
        distance_part(points, row_norms, piv_x.astype(jnp.bfloat16), square_norms(piv_x)),
        contract(prior, piv_factor, True),
    )
    swapped = lax.ppermute(partials, "rank", [(i, i ^ 1) for i in range(rank_count)])
    distance, product = (mine + other for mine, other in zip(partials, swapped))
    matches = (global_ids[:, None] == pivots[None, :]).astype(jnp.float32)
    panel = jnp.exp(-distance / feature_count) + NUGGET * matches - product
    first_full = contract(panel[:, :block], first_inverse, True)
    second_panel = panel[:, block:] - contract(first_full, second_first, True)
    first_columns = lax.dynamic_slice_in_dim(first_full, col_start, col_count, 1)
    second_columns = contract(
        second_panel, lax.dynamic_slice_in_dim(second_inverse, col_start, col_count, 0), True
    )
    return (first_columns, second_columns)


def solution(mesh):
    return jax.shard_map(
        per_device,
        mesh=mesh,
        in_specs=(P("pts", "rank"), P("pts", "rank"), P(), P()),
        out_specs=(P("pts", "rank"), P("pts", "rank")),
        check_vma=False,
    )
```

```python
import jax
import jax.numpy as jnp
from jax import lax
from jax.sharding import PartitionSpec as P

NUGGET = 2.0


def contract(left_rows, right_rows, precise):
    dims = (((1,), (1,)), ((), ()))
    if precise:
        return lax.dot_general(
            left_rows,
            right_rows,
            dims,
            precision=lax.Precision.HIGHEST,
            preferred_element_type=jnp.float32,
        )
    return lax.dot_general(left_rows, right_rows, dims, preferred_element_type=jnp.float32)


def contract_high(left_rows, right_rows):
    return lax.dot_general(
        left_rows,
        right_rows,
        (((1,), (1,)), ((), ())),
        precision=lax.Precision.HIGH,
        preferred_element_type=jnp.float32,
    )


def owned_rows(source, pivots, first_id):
    row_count = source.shape[0]
    local_index = pivots - first_id
    inside = (local_index >= 0) & (local_index < row_count)
    picked = jnp.take(source, jnp.clip(local_index, 0, row_count - 1), axis=0)
    return jnp.where(inside[:, None], picked.astype(jnp.float32), 0.0)


def square_norms(values):
    wide = values.astype(jnp.float32)
    return jnp.sum(wide * wide, axis=1)


def distance_part(left_rows, left_norms, right_rows, right_norms):
    return left_norms[:, None] + right_norms[None, :] - 2.0 * contract(left_rows, right_rows, False)


def inverse_factor(kernel_block):
    size = kernel_block.shape[0]
    half = size // 2
    identity = jnp.eye(half, dtype=jnp.float32)
    upper_factor = jnp.linalg.cholesky(kernel_block[:half, :half])
    upper_inverse = jax.scipy.linalg.solve_triangular(upper_factor, identity, lower=True)
    cross_factor = contract(kernel_block[half:, :half], upper_inverse, True)
    rest = kernel_block[half:, half:] - contract(cross_factor, cross_factor, True)
    lower_factor = jnp.linalg.cholesky(rest)
    lower_inverse = jax.scipy.linalg.solve_triangular(lower_factor, identity, lower=True)
    cross_inverse = -lax.dot_general(
        lower_inverse,
        contract(cross_factor, upper_inverse.T, True),
        (((1,), (0,)), ((), ())),
        precision=lax.Precision.HIGHEST,
        preferred_element_type=jnp.float32,
    )
    zeros = jnp.zeros((half, size - half), jnp.float32)
    return jnp.concatenate(
        [
            jnp.concatenate([upper_inverse, zeros], axis=1),
            jnp.concatenate([cross_inverse, lower_inverse], axis=1),
        ],
        axis=0,
    )


def butterfly_sum(values, steps):
    kept = []
    for axis, shift, radix in steps:
        size = lax.axis_size(axis)
        digit = (lax.axis_index(axis) >> shift) % radix
        chunk = values[0].shape[0] // radix
        received = []
        for t in range(1, radix):
            pairs = [(i, i ^ (t << shift)) for i in range(size)]
            sent = [lax.dynamic_slice_in_dim(v, (digit ^ t) * chunk, chunk, 0) for v in values]
            received.append(lax.ppermute(sent, axis, pairs))
        mine = [lax.dynamic_slice_in_dim(v, digit * chunk, chunk, 0) for v in values]
        for part in received:
            mine = [m + r for m, r in zip(mine, part)]
        values = mine
        kept.append((axis, shift, radix, digit, chunk))
    for axis, shift, radix, digit, chunk in reversed(kept):
        size = lax.axis_size(axis)
        whole = [
            lax.dynamic_update_slice_in_dim(
                jnp.zeros((radix * chunk,) + v.shape[1:], v.dtype), v, digit * chunk, 0
            )
            for v in values
        ]
        for t in range(1, radix):
            pairs = [(i, i ^ (t << shift)) for i in range(size)]
            part = lax.ppermute(values, axis, pairs)
            whole = [
                lax.dynamic_update_slice_in_dim(w, r, (digit ^ t) * chunk, 0)
                for w, r in zip(whole, part)
            ]
        values = whole
    return values


def per_device(points, prior, first_pivots, second_pivots):
    row_count, x_half = points.shape
    f_half = prior.shape[1]
    first_id = lax.axis_index("pts") * row_count
    global_ids = first_id + lax.iota(jnp.int32, row_count)
    rank = lax.axis_index("rank")
    rank_count = lax.axis_size("rank")
    block = first_pivots.shape[0]
    col_count = block // rank_count
    col_start = rank * col_count
    feature_count = x_half * rank_count
    pivots = jnp.concatenate([first_pivots, second_pivots])
    row_norms = square_norms(points)
    select = pivots[:, None] == global_ids[None, :]
    take = (((1,), (0,)), ((), ()))
    x_rows = lax.dot_general(
        select.astype(points.dtype), points, take, preferred_element_type=jnp.float32
    )
    f_rows = lax.dot_general(
        select.astype(jnp.float32),
        prior,
        take,
        precision=lax.Precision.HIGHEST,
        preferred_element_type=jnp.float32,
    )
    x_slot = jnp.zeros((2 * block, feature_count), jnp.float32)
    f_slot = jnp.zeros((2 * block, f_half * rank_count), jnp.float32)
    x_slot = lax.dynamic_update_slice_in_dim(x_slot, x_rows, rank * x_half, 1)
    f_slot = lax.dynamic_update_slice_in_dim(f_slot, f_rows, rank * f_half, 1)
    steps = [("rank", 0, 2), ("pts", 3, 4), ("pts", 5, 4), ("pts", 0, 4), ("pts", 2, 2)]
    (rows_full,) = butterfly_sum([jnp.concatenate([x_slot, f_slot], axis=1)], steps)
    x_full = rows_full[:, :feature_count]
    f_full = rows_full[:, feature_count:]
    x_wide = x_full.astype(jnp.bfloat16)
    full_norms = square_norms(x_full)
    piv_distance = distance_part(x_wide, full_norms, x_wide, full_norms)
    identity = jnp.eye(2 * block, dtype=jnp.float32)
    piv_kernel = jnp.exp(-piv_distance / feature_count) + NUGGET * identity - contract_high(f_full, f_full)
    first_inverse = inverse_factor(piv_kernel[:block, :block])
    second_first = contract(piv_kernel[block:, :block], first_inverse, True)
    second_kernel = piv_kernel[block:, block:] - contract(second_first, second_first, True)
    second_inverse = inverse_factor(second_kernel)
    piv_x = lax.dynamic_slice_in_dim(x_full, rank * x_half, x_half, 1)
    piv_factor = lax.dynamic_slice_in_dim(f_full, rank * f_half, f_half, 1)
    partials = (
        distance_part(points, row_norms, piv_x.astype(jnp.bfloat16), square_norms(piv_x)),
        contract_high(prior, piv_factor),
    )
    swapped = lax.ppermute(partials, "rank", [(i, i ^ 1) for i in range(rank_count)])
    distance, product = (mine + other for mine, other in zip(partials, swapped))
    matches = (global_ids[:, None] == pivots[None, :]).astype(jnp.float32)
    panel = jnp.exp(-distance / feature_count) + NUGGET * matches - product
    first_full = contract(panel[:, :block], first_inverse, True)
    second_panel = panel[:, block:] - contract(first_full, second_first, True)
    first_columns = lax.dynamic_slice_in_dim(first_full, col_start, col_count, 1)
    second_columns = contract(
        second_panel, lax.dynamic_slice_in_dim(second_inverse, col_start, col_count, 0), True
    )
    return (first_columns, second_columns)


def solution(mesh):
    return jax.shard_map(
        per_device,
        mesh=mesh,
        in_specs=(P("pts", "rank"), P("pts", "rank"), P(), P()),
        out_specs=(P("pts", "rank"), P("pts", "rank")),
        check_vma=False,
    )
```

```python
import jax
import jax.numpy as jnp
from jax import lax
from jax.sharding import PartitionSpec as P

NUGGET = 2.0


def contract(left_rows, right_rows, precise):
    dims = (((1,), (1,)), ((), ()))
    if precise:
        return lax.dot_general(
            left_rows,
            right_rows,
            dims,
            precision=lax.Precision.HIGHEST,
            preferred_element_type=jnp.float32,
        )
    return lax.dot_general(left_rows, right_rows, dims, preferred_element_type=jnp.float32)


def contract_high(left_rows, right_rows):
    return lax.dot_general(
        left_rows,
        right_rows,
        (((1,), (1,)), ((), ())),
        precision=lax.Precision.HIGH,
        preferred_element_type=jnp.float32,
    )


def owned_rows(source, pivots, first_id):
    row_count = source.shape[0]
    local_index = pivots - first_id
    inside = (local_index >= 0) & (local_index < row_count)
    picked = jnp.take(source, jnp.clip(local_index, 0, row_count - 1), axis=0)
    return jnp.where(inside[:, None], picked.astype(jnp.float32), 0.0)


def square_norms(values):
    wide = values.astype(jnp.float32)
    return jnp.sum(wide * wide, axis=1)


def distance_part(left_rows, left_norms, right_rows, right_norms):
    return left_norms[:, None] + right_norms[None, :] - 2.0 * contract(left_rows, right_rows, False)


def inverse_factor(kernel_block):
    size = kernel_block.shape[0]
    half = size // 2
    identity = jnp.eye(half, dtype=jnp.float32)
    upper_factor = jnp.linalg.cholesky(kernel_block[:half, :half])
    upper_inverse = jax.scipy.linalg.solve_triangular(upper_factor, identity, lower=True)
    cross_factor = contract(kernel_block[half:, :half], upper_inverse, True)
    rest = kernel_block[half:, half:] - contract(cross_factor, cross_factor, True)
    lower_factor = jnp.linalg.cholesky(rest)
    lower_inverse = jax.scipy.linalg.solve_triangular(lower_factor, identity, lower=True)
    cross_inverse = -lax.dot_general(
        lower_inverse,
        contract(cross_factor, upper_inverse.T, True),
        (((1,), (0,)), ((), ())),
        precision=lax.Precision.HIGHEST,
        preferred_element_type=jnp.float32,
    )
    zeros = jnp.zeros((half, size - half), jnp.float32)
    return jnp.concatenate(
        [
            jnp.concatenate([upper_inverse, zeros], axis=1),
            jnp.concatenate([cross_inverse, lower_inverse], axis=1),
        ],
        axis=0,
    )


def butterfly_sum(values, steps):
    kept = []
    for axis, shift, radix in steps:
        size = lax.axis_size(axis)
        digit = (lax.axis_index(axis) >> shift) % radix
        chunk = values[0].shape[0] // radix
        received = []
        for t in range(1, radix):
            pairs = [(i, i ^ (t << shift)) for i in range(size)]
            sent = [lax.dynamic_slice_in_dim(v, (digit ^ t) * chunk, chunk, 0) for v in values]
            received.append(lax.ppermute(sent, axis, pairs))
        mine = [lax.dynamic_slice_in_dim(v, digit * chunk, chunk, 0) for v in values]
        for part in received:
            mine = [m + r for m, r in zip(mine, part)]
        values = mine
        kept.append((axis, shift, radix, digit, chunk))
    for axis, shift, radix, digit, chunk in reversed(kept):
        size = lax.axis_size(axis)
        whole = [
            lax.dynamic_update_slice_in_dim(
                jnp.zeros((radix * chunk,) + v.shape[1:], v.dtype), v, digit * chunk, 0
            )
            for v in values
        ]
        for t in range(1, radix):
            pairs = [(i, i ^ (t << shift)) for i in range(size)]
            part = lax.ppermute(values, axis, pairs)
            whole = [
                lax.dynamic_update_slice_in_dim(w, r, (digit ^ t) * chunk, 0)
                for w, r in zip(whole, part)
            ]
        values = whole
    return values


def per_device(points, prior, first_pivots, second_pivots):
    row_count, x_half = points.shape
    f_half = prior.shape[1]
    first_id = lax.axis_index("pts") * row_count
    global_ids = first_id + lax.iota(jnp.int32, row_count)
    rank = lax.axis_index("rank")
    rank_count = lax.axis_size("rank")
    block = first_pivots.shape[0]
    col_count = block // rank_count
    col_start = rank * col_count
    feature_count = x_half * rank_count
    pivots = jnp.concatenate([first_pivots, second_pivots])
    row_norms = square_norms(points)
    select = pivots[:, None] == global_ids[None, :]
    take = (((1,), (0,)), ((), ()))
    x_rows = lax.dot_general(
        select.astype(points.dtype), points, take, preferred_element_type=jnp.float32
    )
    f_rows = lax.dot_general(
        select.astype(jnp.float32),
        prior,
        take,
        precision=lax.Precision.HIGHEST,
        preferred_element_type=jnp.float32,
    )
    x_slot = jnp.zeros((2 * block, feature_count), jnp.float32)
    f_slot = jnp.zeros((2 * block, f_half * rank_count), jnp.float32)
    x_slot = lax.dynamic_update_slice_in_dim(x_slot, x_rows, rank * x_half, 1)
    f_slot = lax.dynamic_update_slice_in_dim(f_slot, f_rows, rank * f_half, 1)
    steps = [("rank", 0, 2), ("pts", 3, 4), ("pts", 5, 4), ("pts", 0, 4), ("pts", 2, 2)]
    (rows_full,) = butterfly_sum([jnp.concatenate([x_slot, f_slot], axis=1)], steps)
    x_full = rows_full[:, :feature_count]
    f_full = rows_full[:, feature_count:]
    x_wide = x_full.astype(jnp.bfloat16)
    full_norms = square_norms(x_full)
    piv_distance = distance_part(x_wide, full_norms, x_wide, full_norms)
    identity = jnp.eye(2 * block, dtype=jnp.float32)
    piv_kernel = jnp.exp(-piv_distance / feature_count) + NUGGET * identity - contract_high(f_full, f_full)
    first_inverse = inverse_factor(piv_kernel[:block, :block])
    second_first = contract(piv_kernel[block:, :block], first_inverse, True)
    second_kernel = piv_kernel[block:, block:] - contract(second_first, second_first, True)
    second_inverse = inverse_factor(second_kernel)
    piv_x = lax.dynamic_slice_in_dim(x_full, rank * x_half, x_half, 1)
    piv_factor = lax.dynamic_slice_in_dim(f_full, rank * f_half, f_half, 1)
    partials = (
        distance_part(points, row_norms, piv_x.astype(jnp.bfloat16), square_norms(piv_x)),
        contract_high(prior, piv_factor),
    )
    swapped = lax.ppermute(partials, "rank", [(i, i ^ 1) for i in range(rank_count)])
    distance, product = (mine + other for mine, other in zip(partials, swapped))
    matches = (global_ids[:, None] == pivots[None, :]).astype(jnp.float32)
    panel = jnp.exp(-distance / feature_count) + NUGGET * matches - product
    first_full = contract_high(panel[:, :block], first_inverse)
    second_panel = panel[:, block:] - contract_high(first_full, second_first)
    first_columns = lax.dynamic_slice_in_dim(first_full, col_start, col_count, 1)
    second_columns = contract_high(
        second_panel, lax.dynamic_slice_in_dim(second_inverse, col_start, col_count, 0)
    )
    return (first_columns, second_columns)


def solution(mesh):
    return jax.shard_map(
        per_device,
        mesh=mesh,
        in_specs=(P("pts", "rank"), P("pts", "rank"), P(), P()),
        out_specs=(P("pts", "rank"), P("pts", "rank")),
        check_vma=False,
    )
```
